256 devices in a mesh: dp: 8 (over x_hi, y), seq: 32 (over x_lo, z, core).
Axes of the slice: x: 4 (x_hi: 2, x_lo: 2; x = x_hi * 2 + x_lo), y: 4, z: 8, core: 2. Of those that a mesh axis runs over, the one named last changes fastest.
Arguments:
- tokens: bfloat16 [8, 12288, 2048], P('dp', 'seq'), may hold values from -32 to 32
- w_qkv: bfloat16 [2048, 3072], P(('dp', 'seq')), may hold values from -1 to 1
- w_out: bfloat16 [1024, 2048], P(('dp', 'seq')), may hold values from -0.1875 to 0.1875
Outputs:
- mixed: bfloat16 [8, 12288, 2048], P('dp', 'seq')
The draws below stay inside these ranges and needn't reach their ends.
All inputs are finite; a program needn't handle non-finite values.
Results may differ from the reference program's by a relative error of at most 0.007.
Values may be sent and summed in bfloat16 or wider, within the bound.
No kernel may reach another device: no remote copies, remote signals or barrier semaphores. Data moves between devices by JAX's collectives and lax.ppermute only.
A program may use at most 64 MiB of HBM per device.

```python
import math
import jax
import jax.numpy as jnp
from jax import lax

D = 2048
HEADS = 8
HEAD_DIM = 128
COLS = 96
BATCH = 8
GRID_ROWS = 128
TOKENS = 12288
INNER = 1024


def draw_tokens(key, part):
    keys = jax.random.split(jax.random.fold_in(key, 11), 6)
    values = jax.random.normal(keys[5], (BATCH, TOKENS, D))
    return jnp.clip(values, -32.0, 32.0).astype(jnp.bfloat16)


def draw_w_qkv(key, part):
    keys = jax.random.split(jax.random.fold_in(key, 23), 1)
    weights = jax.random.normal(keys[0], (D, HEADS, 3, HEAD_DIM)) / math.sqrt(D)
    return jnp.clip(weights.reshape(D, HEADS * 3 * HEAD_DIM), -1.0, 1.0).astype(jnp.bfloat16)


def block_scale(stream_key, dims, cuts, least, high):
    loudness = 1.0
    for axis_at, shards_of in cuts:
        heights = jax.random.uniform(jax.random.fold_in(jax.random.fold_in(stream_key, 6), axis_at), (shards_of,), jnp.float32, least / len(cuts), high / len(cuts))
        loudness = loudness * jnp.repeat(jnp.exp(heights), dims[axis_at] // shards_of).reshape((-1,) + (1,) * (len(dims) - 1 - axis_at))
    return loudness


def centred(rng, dims, width, reach, pieces=(), dtype=jnp.bfloat16):
    drawn = width * jax.random.normal(rng, dims, jnp.float32)
    if pieces:
        drawn = drawn * block_scale(rng, dims, pieces, -0.22, 0.18)
    return jnp.clip(drawn, -reach, reach).astype(dtype)


def setup_inputs(seed: int = 0) -> dict:
    key_of = jax.random.split(jax.random.key(seed), 4)
    tokens = draw_tokens(jax.random.fold_in(key_of[3], 71), 0)
    w_qkv = draw_w_qkv(jax.random.fold_in(key_of[3], 71), 0)
    w_out = centred(key_of[2], (INNER, D), INNER ** -0.5, 0.1875, ((0, 256),))
    return {"tokens": tokens, "w_qkv": w_qkv, "w_out": w_out}


def attend(query, keys, values, allowed):
    scores = jnp.einsum('bhqd,bhkd->bhqk', query.astype(jnp.float32), keys.astype(jnp.float32)) / math.sqrt(query.shape[-1])
    scores = jnp.where(allowed, scores, -jnp.inf)
    top = lax.optimization_barrier(jnp.max(scores, axis=-1, keepdims=True))
    expo = jnp.exp(scores - top)
    weights = (expo / lax.optimization_barrier(jnp.sum(expo, axis=-1, keepdims=True))).astype(jnp.bfloat16)
    return jnp.einsum('bhqk,bhkd->bhqd', weights.astype(jnp.float32), values.astype(jnp.float32)).astype(jnp.bfloat16)

def reference(tokens, w_qkv, w_out):
    half = HEADS // 2

    def one_sequence(sequence):
        qkv = jnp.dot(sequence, w_qkv, preferred_element_type=jnp.float32).astype(jnp.bfloat16)
        qkv = qkv.reshape(GRID_ROWS, COLS, HEADS, 3, HEAD_DIM)
        col_places = jnp.arange(COLS)
        row_places = jnp.arange(GRID_ROWS)
        row_mask = col_places[:, None] >= col_places[None, :]
        col_mask = row_places[:, None] >= row_places[None, :]
        row_part = jnp.transpose(qkv[:, :, :half], (0, 2, 3, 1, 4))
        row_out = attend(row_part[:, :, 0], row_part[:, :, 1], row_part[:, :, 2], row_mask)
        row_out = jnp.transpose(row_out, (0, 2, 1, 3))
        col_part = jnp.transpose(qkv[:, :, half:], (1, 2, 3, 0, 4))
        col_out = attend(col_part[:, :, 0], col_part[:, :, 1], col_part[:, :, 2], col_mask)
        col_out = jnp.transpose(col_out, (2, 0, 1, 3))
        heads_out = jnp.concatenate([row_out, col_out], axis=2).reshape(TOKENS, HEADS * HEAD_DIM)
        return jnp.dot(heads_out, w_out, preferred_element_type=jnp.float32).astype(jnp.bfloat16)
    return lax.map(one_sequence, tokens)
```

```python
import math

import jax
import jax.numpy as jnp
from jax import lax
from jax.sharding import Mesh
from jax.sharding import PartitionSpec as P

HEADS = 8
HEAD_DIM = 128
COLS = 96
AXES = ("xh", "y", "xl", "z", "c")
SPLIT = (2, 4, 2, 8, 2)
X = ("xh", "xl")
SEQ = ("xl", "z", "c")


def ring(block, axis, n):
    idx = lax.axis_index(axis)
    buf = jnp.zeros((n,) + block.shape, block.dtype)
    buf = lax.dynamic_update_index_in_dim(buf, block, idx, 0)
    fwd = bwd = block
    for s in range(1, n // 2 + 1):
        fwd = lax.ppermute(fwd, axis, [(i, (i + 1) % n) for i in range(n)])
        buf = lax.dynamic_update_index_in_dim(buf, fwd, (idx + n - s) % n, 0)
        if s < n - s:
            bwd = lax.ppermute(bwd, axis, [(i, (i - 1) % n) for i in range(n)])
            buf = lax.dynamic_update_index_in_dim(buf, bwd, (idx + s) % n, 0)
    return buf


def gather_rows(w):
    own = ring(ring(ring(w, "z", 8), "y", 4), X, 4)
    other = lax.ppermute(own, "c", [(0, 1), (1, 0)])
    rows = own.shape[0] * own.shape[1] * own.shape[2] * own.shape[3]
    return own.reshape(rows, w.shape[1]), other.reshape(rows, w.shape[1])


def by_core(left, per_device):
    t = left.reshape(left.shape[0], *SPLIT, per_device)
    t = jnp.transpose(t, (0, 5, 1, 3, 2, 4, 6))
    t = t.reshape(left.shape[0], 2, -1)
    c = lax.axis_index("c")
    own = lax.dynamic_index_in_dim(t, c, 1, keepdims=False)
    other = lax.dynamic_index_in_dim(t, 1 - c, 1, keepdims=False)
    return own, other


def project(left, w_local, gathered):
    own_w, other_w = gathered
    own, other = by_core(left, w_local.shape[0])
    return jnp.dot(own, own_w, preferred_element_type=jnp.float32) + jnp.dot(
        other, other_w, preferred_element_type=jnp.float32
    )


def attend(query, keys, values, allowed):
    scores = jnp.einsum(
        "shqd,shkd->shqk", query, keys, preferred_element_type=jnp.float32
    ) / math.sqrt(query.shape[-1])
    scores = jnp.where(allowed, scores, -jnp.inf)
    top = jnp.max(scores, axis=-1, keepdims=True)
    expo = jnp.exp(scores - top)
    weights = (expo / jnp.sum(expo, axis=-1, keepdims=True)).astype(jnp.bfloat16)
    return jnp.einsum(
        "shqk,shkd->shqd", weights, values, preferred_element_type=jnp.float32
    ).astype(jnp.bfloat16)


def column_heads(packed):
    seq_count, grid_rows, local_cols, count, width = packed.shape
    length = grid_rows * local_cols
    flat = packed.reshape(seq_count, length, count, 3, width // 3)
    flat = jnp.transpose(flat, (0, 2, 3, 1, 4))
    places = jnp.arange(length)
    allowed = (places[:, None] % local_cols == places[None, :] % local_cols) & (
        places[:, None] >= places[None, :]
    )
    result = attend(flat[:, :, 0], flat[:, :, 1], flat[:, :, 2], allowed)
    result = jnp.transpose(result, (0, 2, 1, 3)).reshape(
        seq_count, grid_rows, local_cols, count, width // 3
    )
    return lax.all_to_all(result, SEQ, split_axis=1, concat_axis=2, tiled=True)


def on_device(tokens, w_qkv, w_out):
    seq_count, tok_count, width = tokens.shape
    flat = tokens.reshape(seq_count * tok_count, width)
    half = HEADS // 2
    qkv_w = gather_rows(w_qkv)
    out_w = gather_rows(w_out)
    qkv = project(flat, w_qkv, qkv_w)
    qkv = qkv.astype(jnp.bfloat16).reshape(seq_count, tok_count, HEADS, 3, HEAD_DIM)
    col_packed = qkv[:, :, half:].reshape(seq_count, tok_count // COLS, COLS, half, 3 * HEAD_DIM)
    col_out = column_heads(
        lax.all_to_all(col_packed, SEQ, split_axis=2, concat_axis=1, tiled=True)
    )
    col_out = col_out.reshape(seq_count, tok_count, half, HEAD_DIM)
    row_part = jnp.transpose(qkv[:, :, :half], (0, 2, 3, 1, 4))
    places = jnp.arange(tok_count)
    row_mask = (places[:, None] // COLS == places[None, :] // COLS) & (
        places[:, None] >= places[None, :]
    )
    row_out = attend(row_part[:, :, 0], row_part[:, :, 1], row_part[:, :, 2], row_mask)
    row_out = jnp.transpose(row_out, (0, 2, 1, 3))
    heads_out = jnp.concatenate([row_out, col_out], axis=2).reshape(
        seq_count * tok_count, HEADS * HEAD_DIM
    )
    mixed = project(heads_out, w_out, out_w)
    return mixed.astype(jnp.bfloat16).reshape(seq_count, tok_count, w_out.shape[1])


def solution(mesh):
    grid = Mesh(mesh.devices.reshape(SPLIT), AXES)
    act = P(("xh", "y"), SEQ, None)
    weight = P(AXES, None)
    return jax.shard_map(
        on_device, mesh=grid, in_specs=(act, weight, weight), out_specs=act, check_vma=False
    )
```

```python
import math

import jax
import jax.numpy as jnp
from jax import lax
from jax.sharding import Mesh
from jax.sharding import PartitionSpec as P

HEADS = 8
HEAD_DIM = 128
COLS = 96
AXES = ("xh", "y", "xl", "z", "c")
SPLIT = (2, 4, 2, 8, 2)
X = ("xh", "xl")
SEQ = ("xl", "z", "c")


def ring(block, axis, n):
    idx = lax.axis_index(axis)
    buf = jnp.zeros((n,) + block.shape, block.dtype)
    buf = lax.dynamic_update_index_in_dim(buf, block, idx, 0)
    fwd = bwd = block
    for s in range(1, n // 2 + 1):
        fwd = lax.ppermute(fwd, axis, [(i, (i + 1) % n) for i in range(n)])
        buf = lax.dynamic_update_index_in_dim(buf, fwd, (idx + n - s) % n, 0)
        if s < n - s:
            bwd = lax.ppermute(bwd, axis, [(i, (i - 1) % n) for i in range(n)])
            buf = lax.dynamic_update_index_in_dim(buf, bwd, (idx + s) % n, 0)
    return buf


DIMS = {"xh": (1,), "y": (2,), "xl": (3,), "z": (4,), X: (1, 3)}
ORDERS = (("z", "y", X), ("y", X, "z"), (X, "z", "y"))
SIZE = {"z": 8, "y": 4, X: 4}


def gather_rows(w, order):
    own = w
    for axis in order:
        own = ring(own, axis, SIZE[axis])
    other = lax.ppermute(own, "c", [(0, 1), (1, 0)])
    rows = own.size // w.shape[1]
    return own.reshape(rows, w.shape[1]), other.reshape(rows, w.shape[1])


def by_core(left, per_device, order):
    t = left.reshape(left.shape[0], *SPLIT, per_device)
    inner = tuple(d for axis in reversed(order) for d in DIMS[axis])
    t = jnp.transpose(t, (0, 5) + inner + (6,))
    t = t.reshape(left.shape[0], 2, -1)
    c = lax.axis_index("c")
    own = lax.dynamic_index_in_dim(t, c, 1, keepdims=False)
    other = lax.dynamic_index_in_dim(t, 1 - c, 1, keepdims=False)
    return own, other


def project(left, per_device, gathered, order):
    own_w, other_w = gathered
    own, other = by_core(left, per_device, order)
    return jnp.dot(own, own_w, preferred_element_type=jnp.float32) + jnp.dot(
        other, other_w, preferred_element_type=jnp.float32
    )


def attend(query, keys, values, allowed):
    scores = jnp.einsum(
        "shqd,shkd->shqk", query, keys, preferred_element_type=jnp.float32
    ) / math.sqrt(query.shape[-1])
    scores = jnp.where(allowed, scores, -jnp.inf)
    top = jnp.max(scores, axis=-1, keepdims=True)
    expo = jnp.exp(scores - top)
    weights = (expo / jnp.sum(expo, axis=-1, keepdims=True)).astype(jnp.bfloat16)
    return jnp.einsum(
        "shqk,shkd->shqd", weights, values, preferred_element_type=jnp.float32
    ).astype(jnp.bfloat16)


def column_heads(packed):
    seq_count, grid_rows, local_cols, count, width = packed.shape
    length = grid_rows * local_cols
    flat = packed.reshape(seq_count, length, count, 3, width // 3)
    flat = jnp.transpose(flat, (0, 2, 3, 1, 4))
    places = jnp.arange(length)
    allowed = (places[:, None] % local_cols == places[None, :] % local_cols) & (
        places[:, None] >= places[None, :]
    )
    result = attend(flat[:, :, 0], flat[:, :, 1], flat[:, :, 2], allowed)
    result = jnp.transpose(result, (0, 2, 1, 3)).reshape(
        seq_count, grid_rows, local_cols, count, width // 3
    )
    return lax.all_to_all(result, SEQ, split_axis=1, concat_axis=2, tiled=True)


def on_device(tokens, w_qkv, w_out):
    seq_count, tok_count, width = tokens.shape
    flat = tokens.reshape(seq_count * tok_count, width)
    half = HEADS // 2
    parts = len(ORDERS)
    step = w_qkv.shape[1] // parts
    pieces = [
        gather_rows(w_qkv[:, p * step:(p + 1) * step], order)
        for p, order in enumerate(ORDERS)
    ]
    qkv = jnp.concatenate(
        [project(flat, w_qkv.shape[0], g, order) for g, order in zip(pieces, ORDERS)],
        axis=1,
    ).astype(jnp.bfloat16)
    w_out, qkv = lax.optimization_barrier((w_out, qkv))
    out_w = gather_rows(w_out, ORDERS[0])
    qkv = qkv.reshape(seq_count, tok_count, HEADS, 3, HEAD_DIM)
    col_packed = qkv[:, :, half:].reshape(seq_count, tok_count // COLS, COLS, half, 3 * HEAD_DIM)
    col_out = column_heads(
        lax.all_to_all(col_packed, SEQ, split_axis=2, concat_axis=1, tiled=True)
    )
    col_out = col_out.reshape(seq_count, tok_count, half, HEAD_DIM)
    row_part = jnp.transpose(qkv[:, :, :half], (0, 2, 3, 1, 4))
    places = jnp.arange(tok_count)
    row_mask = (places[:, None] // COLS == places[None, :] // COLS) & (
        places[:, None] >= places[None, :]
    )
    row_out = attend(row_part[:, :, 0], row_part[:, :, 1], row_part[:, :, 2], row_mask)
    row_out = jnp.transpose(row_out, (0, 2, 1, 3))
    heads_out = jnp.concatenate([row_out, col_out], axis=2).reshape(
        seq_count * tok_count, HEADS * HEAD_DIM
    )
    mixed = project(heads_out, w_out.shape[0], out_w, ORDERS[0])
    return mixed.astype(jnp.bfloat16).reshape(seq_count, tok_count, w_out.shape[1])


def solution(mesh):
    grid = Mesh(mesh.devices.reshape(SPLIT), AXES)
    act = P(("xh", "y"), SEQ, None)
    weight = P(AXES, None)
    return jax.shard_map(
        on_device, mesh=grid, in_specs=(act, weight, weight), out_specs=act, check_vma=False
    )
```

```python
import math

import jax
import jax.numpy as jnp
from jax import lax
from jax.sharding import Mesh
from jax.sharding import PartitionSpec as P

HEADS = 8
HEAD_DIM = 128
COLS = 96
AXES = ("xh", "y", "xl", "z", "c")
SPLIT = (2, 4, 2, 8, 2)
X = ("xh", "xl")
SEQ = ("xl", "z", "c")


def ring(block, axis, n):
    idx = lax.axis_index(axis)
    buf = jnp.zeros((n,) + block.shape, block.dtype)
    buf = lax.dynamic_update_index_in_dim(buf, block, idx, 0)
    fwd = bwd = block
    for s in range(1, n // 2 + 1):
        fwd = lax.ppermute(fwd, axis, [(i, (i + 1) % n) for i in range(n)])
        buf = lax.dynamic_update_index_in_dim(buf, fwd, (idx + n - s) % n, 0)
        if s < n - s:
            bwd = lax.ppermute(bwd, axis, [(i, (i - 1) % n) for i in range(n)])
            buf = lax.dynamic_update_index_in_dim(buf, bwd, (idx + s) % n, 0)
    return buf


DIMS = {"xh": (1,), "y": (2,), "xl": (3,), "z": (4,), X: (1, 3)}
PLANS = ((("y", "z"), X), (("xh", "xl", "z"), "y"))
SIZE = {"y": 4, X: 4}


def gather_rows(w, plan):
    group, axis = plan
    n = 1
    for name in group:
        n *= SPLIT[AXES.index(name)]
    spread = jnp.broadcast_to(w[None], (n,) + w.shape)
    own = lax.all_to_all(spread, group, 0, 0, tiled=True)
    own = ring(own, axis, SIZE[axis])
    other = lax.ppermute(own, "c", [(0, 1), (1, 0)])
    rows = own.size // w.shape[1]
    return own.reshape(rows, w.shape[1]), other.reshape(rows, w.shape[1])


def order_of(plan):
    group, axis = plan
    inner = tuple(X if name == "xl" else name for name in group if name != "xh")
    return (axis,) + inner


def by_core(left, per_device, order):
    t = left.reshape(left.shape[0], *SPLIT, per_device)
    inner = tuple(d for axis in order_of(order) for d in DIMS[axis])
    t = jnp.transpose(t, (0, 5) + inner + (6,))
    t = t.reshape(left.shape[0], 2, -1)
    c = lax.axis_index("c")
    own = lax.dynamic_index_in_dim(t, c, 1, keepdims=False)
    other = lax.dynamic_index_in_dim(t, 1 - c, 1, keepdims=False)
    return own, other


def project(left, per_device, gathered, order):
    own_w, other_w = gathered
    own, other = by_core(left, per_device, order)
    return jnp.dot(own, own_w, preferred_element_type=jnp.float32) + jnp.dot(
        other, other_w, preferred_element_type=jnp.float32
    )


def attend(query, keys, values, allowed):
    scores = jnp.einsum(
        "shqd,shkd->shqk", query, keys, preferred_element_type=jnp.float32
    ) / math.sqrt(query.shape[-1])
    scores = jnp.where(allowed, scores, -jnp.inf)
    top = jnp.max(scores, axis=-1, keepdims=True)
    expo = jnp.exp(scores - top)
    weights = (expo / jnp.sum(expo, axis=-1, keepdims=True)).astype(jnp.bfloat16)
    return jnp.einsum(
        "shqk,shkd->shqd", weights, values, preferred_element_type=jnp.float32
    ).astype(jnp.bfloat16)


def column_heads(packed):
    seq_count, grid_rows, local_cols, count, width = packed.shape
    length = grid_rows * local_cols
    flat = packed.reshape(seq_count, length, count, 3, width // 3)
    flat = jnp.transpose(flat, (0, 2, 3, 1, 4))
    places = jnp.arange(length)
    allowed = (places[:, None] % local_cols == places[None, :] % local_cols) & (
        places[:, None] >= places[None, :]
    )
    result = attend(flat[:, :, 0], flat[:, :, 1], flat[:, :, 2], allowed)
    result = jnp.transpose(result, (0, 2, 1, 3)).reshape(
        seq_count, grid_rows, local_cols, count, width // 3
    )
    return lax.all_to_all(result, SEQ, split_axis=1, concat_axis=2, tiled=True)


def on_device(tokens, w_qkv, w_out):
    seq_count, tok_count, width = tokens.shape
    flat = tokens.reshape(seq_count * tok_count, width)
    half = HEADS // 2
    parts = len(PLANS)
    step = w_qkv.shape[1] // parts
    pieces = [
        gather_rows(w_qkv[:, p * step:(p + 1) * step], order)
        for p, order in enumerate(PLANS)
    ]
    qkv = jnp.concatenate(
        [project(flat, w_qkv.shape[0], g, order) for g, order in zip(pieces, PLANS)],
        axis=1,
    ).astype(jnp.bfloat16)
    w_out, qkv = lax.optimization_barrier((w_out, qkv))
    out_w = gather_rows(w_out, PLANS[0])
    qkv = qkv.reshape(seq_count, tok_count, HEADS, 3, HEAD_DIM)
    col_packed = qkv[:, :, half:].reshape(seq_count, tok_count // COLS, COLS, half, 3 * HEAD_DIM)
    col_out = column_heads(
        lax.all_to_all(col_packed, SEQ, split_axis=2, concat_axis=1, tiled=True)
    )
    col_out = col_out.reshape(seq_count, tok_count, half, HEAD_DIM)
    row_part = jnp.transpose(qkv[:, :, :half], (0, 2, 3, 1, 4))
    places = jnp.arange(tok_count)
    row_mask = (places[:, None] // COLS == places[None, :] // COLS) & (
        places[:, None] >= places[None, :]
    )
    row_out = attend(row_part[:, :, 0], row_part[:, :, 1], row_part[:, :, 2], row_mask)
    row_out = jnp.transpose(row_out, (0, 2, 1, 3))
    heads_out = jnp.concatenate([row_out, col_out], axis=2).reshape(
        seq_count * tok_count, HEADS * HEAD_DIM
    )
    mixed = project(heads_out, w_out.shape[0], out_w, PLANS[0])
    return mixed.astype(jnp.bfloat16).reshape(seq_count, tok_count, w_out.shape[1])


def solution(mesh):
    grid = Mesh(mesh.devices.reshape(SPLIT), AXES)
    act = P(("xh", "y"), SEQ, None)
    weight = P(AXES, None)
    return jax.shard_map(
        on_device, mesh=grid, in_specs=(act, weight, weight), out_specs=act, check_vma=False
    )
```

```python
import math

import jax
import jax.numpy as jnp
from jax import lax
from jax.sharding import Mesh
from jax.sharding import PartitionSpec as P

HEADS = 8
HEAD_DIM = 128
COLS = 96
AXES = ("xh", "y", "xl", "z", "c")
SPLIT = (2, 4, 2, 8, 2)
X = ("xh", "xl")
SEQ = ("xl", "z", "c")


def ring(block, axis, n):
    idx = lax.axis_index(axis)
    buf = jnp.zeros((n,) + block.shape, block.dtype)
    buf = lax.dynamic_update_index_in_dim(buf, block, idx, 0)
    fwd = bwd = block
    for s in range(1, n // 2 + 1):
        fwd = lax.ppermute(fwd, axis, [(i, (i + 1) % n) for i in range(n)])
        buf = lax.dynamic_update_index_in_dim(buf, fwd, (idx + n - s) % n, 0)
        if s < n - s:
            bwd = lax.ppermute(bwd, axis, [(i, (i - 1) % n) for i in range(n)])
            buf = lax.dynamic_update_index_in_dim(buf, bwd, (idx + s) % n, 0)
    return buf


DIMS = {"y": (2,), "z": (4,), X: (1, 3)}
SIZE = {"z": 8, "y": 4, X: 4}
PARTS = (("y", X), (X, "y"))


def rings(buf, axes):
    for axis in axes:
        buf = ring(buf, axis, SIZE[axis])
    return buf


def with_other(own, cols):
    other = lax.ppermute(own, "c", [(0, 1), (1, 0)])
    return own.reshape(-1, cols), other.reshape(-1, cols)


def order_of(axes):
    return tuple(reversed(axes))


def by_core(left, per_device, order):
    t = left.reshape(left.shape[0], *SPLIT, per_device)
    inner = tuple(d for axis in order for d in DIMS[axis])
    t = jnp.transpose(t, (0, 5) + inner + (6,))
    t = t.reshape(left.shape[0], 2, -1)
    c = lax.axis_index("c")
    own = lax.dynamic_index_in_dim(t, c, 1, keepdims=False)
    other = lax.dynamic_index_in_dim(t, 1 - c, 1, keepdims=False)
    return own, other


def project(left, per_device, gathered, order):
    own_w, other_w = gathered
    own, other = by_core(left, per_device, order)
    return jnp.dot(own, own_w, preferred_element_type=jnp.float32) + jnp.dot(
        other, other_w, preferred_element_type=jnp.float32
    )


def attend(query, keys, values, allowed):
    scores = jnp.einsum(
        "shqd,shkd->shqk", query, keys, preferred_element_type=jnp.float32
    ) / math.sqrt(query.shape[-1])
    scores = jnp.where(allowed, scores, -jnp.inf)
    top = jnp.max(scores, axis=-1, keepdims=True)
    expo = jnp.exp(scores - top)
    weights = (expo / jnp.sum(expo, axis=-1, keepdims=True)).astype(jnp.bfloat16)
    return jnp.einsum(
        "shqk,shkd->shqd", weights, values, preferred_element_type=jnp.float32
    ).astype(jnp.bfloat16)


def column_heads(packed):
    seq_count, grid_rows, local_cols, count, width = packed.shape
    length = grid_rows * local_cols
    flat = packed.reshape(seq_count, length, count, 3, width // 3)
    flat = jnp.transpose(flat, (0, 2, 3, 1, 4))
    places = jnp.arange(length)
    allowed = (places[:, None] % local_cols == places[None, :] % local_cols) & (
        places[:, None] >= places[None, :]
    )
    result = attend(flat[:, :, 0], flat[:, :, 1], flat[:, :, 2], allowed)
    result = jnp.transpose(result, (0, 2, 1, 3)).reshape(
        seq_count, grid_rows, local_cols, count, width // 3
    )
    return lax.all_to_all(result, SEQ, split_axis=1, concat_axis=2, tiled=True)


def on_device(tokens, w_qkv, w_out):
    seq_count, tok_count, width = tokens.shape
    flat = tokens.reshape(seq_count * tok_count, width)
    half = HEADS // 2
    along_z = ring(w_qkv, "z", SIZE["z"])
    step = w_qkv.shape[1] // len(PARTS)
    pieces = []
    for p, axes in enumerate(PARTS):
        cols = along_z[..., p * step:(p + 1) * step]
        gathered = with_other(rings(cols, axes), step)
        pieces.append(project(flat, w_qkv.shape[0], gathered, order_of(("z",) + axes)))
    qkv = jnp.concatenate(pieces, axis=1).astype(jnp.bfloat16)
    w_out, qkv = lax.optimization_barrier((w_out, qkv))
    out_axes = ("z", "y", X)
    out_w = with_other(rings(w_out, out_axes), w_out.shape[1])
    qkv = qkv.reshape(seq_count, tok_count, HEADS, 3, HEAD_DIM)
    col_packed = qkv[:, :, half:].reshape(seq_count, tok_count // COLS, COLS, half, 3 * HEAD_DIM)
    col_out = column_heads(
        lax.all_to_all(col_packed, SEQ, split_axis=2, concat_axis=1, tiled=True)
    )
    col_out = col_out.reshape(seq_count, tok_count, half, HEAD_DIM)
    row_part = jnp.transpose(qkv[:, :, :half], (0, 2, 3, 1, 4))
    places = jnp.arange(tok_count)
    row_mask = (places[:, None] // COLS == places[None, :] // COLS) & (
        places[:, None] >= places[None, :]
    )
    row_out = attend(row_part[:, :, 0], row_part[:, :, 1], row_part[:, :, 2], row_mask)
    row_out = jnp.transpose(row_out, (0, 2, 1, 3))
    heads_out = jnp.concatenate([row_out, col_out], axis=2).reshape(
        seq_count * tok_count, HEADS * HEAD_DIM
    )
    mixed = project(heads_out, w_out.shape[0], out_w, order_of(out_axes))
    return mixed.astype(jnp.bfloat16).reshape(seq_count, tok_count, w_out.shape[1])


def solution(mesh):
    grid = Mesh(mesh.devices.reshape(SPLIT), AXES)
    act = P(("xh", "y"), SEQ, None)
    weight = P(AXES, None)
    return jax.shard_map(
        on_device, mesh=grid, in_specs=(act, weight, weight), out_specs=act, check_vma=False
    )
```

```python
import math

import jax
import jax.numpy as jnp
from jax import lax
from jax.sharding import Mesh
from jax.sharding import PartitionSpec as P

HEADS = 8
HEAD_DIM = 128
COLS = 96
AXES = ("xh", "y", "xl", "z", "c")
SPLIT = (2, 4, 2, 8, 2)
X = ("xh", "xl")
SEQ = ("xl", "z", "c")


def ring(block, axis, n):
    idx = lax.axis_index(axis)
    buf = jnp.zeros((n,) + block.shape, block.dtype)
    buf = lax.dynamic_update_index_in_dim(buf, block, idx, 0)
    fwd = bwd = block
    for s in range(1, n // 2 + 1):
        fwd = lax.ppermute(fwd, axis, [(i, (i + 1) % n) for i in range(n)])
        buf = lax.dynamic_update_index_in_dim(buf, fwd, (idx + n - s) % n, 0)
        if s < n - s:
            bwd = lax.ppermute(bwd, axis, [(i, (i - 1) % n) for i in range(n)])
            buf = lax.dynamic_update_index_in_dim(buf, bwd, (idx + s) % n, 0)
    return buf


DIMS = {"y": (2,), "z": (4,), X: (1, 3)}
SIZE = {"z": 8, "y": 4, X: 4}
PARTS = (("y", X), (X, "y"))


def rings(buf, axes):
    for axis in axes:
        buf = ring(buf, axis, SIZE[axis])
    return buf


def with_other(own):
    return own, lax.ppermute(own, "c", [(0, 1), (1, 0)])


def flat_rows(pair, cols):
    return tuple(a.reshape(-1, cols) for a in pair)


def order_of(axes):
    return tuple(reversed(axes))


def by_core(left, per_device, order):
    t = left.reshape(left.shape[0], *SPLIT, per_device)
    inner = tuple(d for axis in order for d in DIMS[axis])
    t = jnp.transpose(t, (0, 5) + inner + (6,))
    t = t.reshape(left.shape[0], 2, -1)
    c = lax.axis_index("c")
    own = lax.dynamic_index_in_dim(t, c, 1, keepdims=False)
    other = lax.dynamic_index_in_dim(t, 1 - c, 1, keepdims=False)
    return own, other


def project(left, per_device, gathered, order):
    own_w, other_w = gathered
    own, other = by_core(left, per_device, order)
    return jnp.dot(own, own_w, preferred_element_type=jnp.float32) + jnp.dot(
        other, other_w, preferred_element_type=jnp.float32
    )


def attend(query, keys, values, allowed):
    scores = jnp.einsum(
        "shqd,shkd->shqk", query, keys, preferred_element_type=jnp.float32
    ) / math.sqrt(query.shape[-1])
    scores = jnp.where(allowed, scores, -jnp.inf)
    top = jnp.max(scores, axis=-1, keepdims=True)
    expo = jnp.exp(scores - top)
    weights = (expo / jnp.sum(expo, axis=-1, keepdims=True)).astype(jnp.bfloat16)
    return jnp.einsum(
        "shqk,shkd->shqd", weights, values, preferred_element_type=jnp.float32
    ).astype(jnp.bfloat16)


def column_heads(packed):
    seq_count, grid_rows, local_cols, count, width = packed.shape
    length = grid_rows * local_cols
    flat = packed.reshape(seq_count, length, count, 3, width // 3)
    flat = jnp.transpose(flat, (0, 2, 3, 1, 4))
    places = jnp.arange(length)
    allowed = (places[:, None] % local_cols == places[None, :] % local_cols) & (
        places[:, None] >= places[None, :]
    )
    result = attend(flat[:, :, 0], flat[:, :, 1], flat[:, :, 2], allowed)
    result = jnp.transpose(result, (0, 2, 1, 3)).reshape(
        seq_count, grid_rows, local_cols, count, width // 3
    )
    return lax.all_to_all(result, SEQ, split_axis=1, concat_axis=2, tiled=True)


def on_device(tokens, w_qkv, w_out):
    seq_count, tok_count, width = tokens.shape
    flat = tokens.reshape(seq_count * tok_count, width)
    half = HEADS // 2
    packed = w_out.reshape(w_qkv.shape[0], -1)
    both = jnp.concatenate([w_qkv, packed], axis=1)
    along_z = ring(both, "z", SIZE["z"])
    step = both.shape[1] // len(PARTS)
    spare = both.shape[1] - w_qkv.shape[1]
    pieces, tail = [], None
    for p, axes in enumerate(PARTS):
        own, other = with_other(rings(along_z[..., p * step:(p + 1) * step], axes))
        order = order_of(("z",) + axes)
        if p == len(PARTS) - 1:
            width = step - spare
            tail = (own[..., width:], other[..., width:]), order
            own, other = own[..., :width], other[..., :width]
        gathered = flat_rows((own, other), own.shape[-1])
        pieces.append(project(flat, w_qkv.shape[0], gathered, order))
    qkv = jnp.concatenate(pieces, axis=1).astype(jnp.bfloat16)
    (out_own, out_other), out_order = tail
    lead = out_own.shape[:-2]
    out_w = tuple(
        a.reshape(*lead, w_out.shape[0], w_out.shape[1]).reshape(-1, w_out.shape[1])
        for a in (out_own, out_other)
    )
    qkv = qkv.reshape(seq_count, tok_count, HEADS, 3, HEAD_DIM)
    col_packed = qkv[:, :, half:].reshape(seq_count, tok_count // COLS, COLS, half, 3 * HEAD_DIM)
    col_out = column_heads(
        lax.all_to_all(col_packed, SEQ, split_axis=2, concat_axis=1, tiled=True)
    )
    col_out = col_out.reshape(seq_count, tok_count, half, HEAD_DIM)
    row_part = jnp.transpose(qkv[:, :, :half], (0, 2, 3, 1, 4))
    places = jnp.arange(tok_count)
    row_mask = (places[:, None] // COLS == places[None, :] // COLS) & (
        places[:, None] >= places[None, :]
    )
    row_out = attend(row_part[:, :, 0], row_part[:, :, 1], row_part[:, :, 2], row_mask)
    row_out = jnp.transpose(row_out, (0, 2, 1, 3))
    heads_out = jnp.concatenate([row_out, col_out], axis=2).reshape(
        seq_count * tok_count, HEADS * HEAD_DIM
    )
    mixed = project(heads_out, w_out.shape[0], out_w, out_order)
    return mixed.astype(jnp.bfloat16).reshape(seq_count, tok_count, w_out.shape[1])


def solution(mesh):
    grid = Mesh(mesh.devices.reshape(SPLIT), AXES)
    act = P(("xh", "y"), SEQ, None)
    weight = P(AXES, None)
    return jax.shard_map(
        on_device, mesh=grid, in_specs=(act, weight, weight), out_specs=act, check_vma=False
    )
```

```python
import math

import jax
import jax.numpy as jnp
from jax import lax
from jax.sharding import Mesh
from jax.sharding import PartitionSpec as P

HEADS = 8
HEAD_DIM = 128
COLS = 96
AXES = ("xh", "y", "xl", "z", "c")
SPLIT = (2, 4, 2, 8, 2)
X = ("xh", "xl")
SEQ = ("xl", "z", "c")


def ring(block, axis, n):
    idx = lax.axis_index(axis)
    buf = jnp.zeros((n,) + block.shape, block.dtype)
    buf = lax.dynamic_update_index_in_dim(buf, block, idx, 0)
    fwd = bwd = block
    for s in range(1, n // 2 + 1):
        fwd = lax.ppermute(fwd, axis, [(i, (i + 1) % n) for i in range(n)])
        buf = lax.dynamic_update_index_in_dim(buf, fwd, (idx + n - s) % n, 0)
        if s < n - s:
            bwd = lax.ppermute(bwd, axis, [(i, (i - 1) % n) for i in range(n)])
            buf = lax.dynamic_update_index_in_dim(buf, bwd, (idx + s) % n, 0)
    return buf


DIMS = {"y": (2,), "z": (4,), X: (1, 3)}
SIZE = {"z": 8, "y": 4, X: 4}
PARTS = (("y", X), (X, "y"))


def rings(buf, axes):
    for axis in axes:
        buf = ring(buf, axis, SIZE[axis])
    return buf


def with_other(own):
    return own, lax.ppermute(own, "c", [(0, 1), (1, 0)])


def flat_rows(pair, cols):
    return tuple(a.reshape(-1, cols) for a in pair)


def order_of(axes):
    return tuple(reversed(axes))


def by_core(left, per_device, order):
    t = left.reshape(left.shape[0], *SPLIT, per_device)
    inner = tuple(d for axis in order for d in DIMS[axis])
    t = jnp.transpose(t, (0, 5) + inner + (6,))
    t = t.reshape(left.shape[0], 2, -1)
    c = lax.axis_index("c")
    own = lax.dynamic_index_in_dim(t, c, 1, keepdims=False)
    other = lax.dynamic_index_in_dim(t, 1 - c, 1, keepdims=False)
    return own, other


def project(left, per_device, gathered, order):
    own_w, other_w = gathered
    own, other = by_core(left, per_device, order)
    return jnp.dot(own, own_w, preferred_element_type=jnp.float32) + jnp.dot(
        other, other_w, preferred_element_type=jnp.float32
    )


def attend(query, keys, values, allowed):
    scores = jnp.einsum(
        "shqd,shkd->shqk", query, keys, preferred_element_type=jnp.float32
    ) / math.sqrt(query.shape[-1])
    scores = jnp.where(allowed, scores, -jnp.inf)
    top = jnp.max(scores, axis=-1, keepdims=True)
    expo = jnp.exp(scores - top)
    weights = (expo / jnp.sum(expo, axis=-1, keepdims=True)).astype(jnp.bfloat16)
    return jnp.einsum(
        "shqk,shkd->shqd", weights, values, preferred_element_type=jnp.float32
    ).astype(jnp.bfloat16)


def column_heads(packed):
    seq_count, grid_rows, local_cols, count, width = packed.shape
    length = grid_rows * local_cols
    flat = packed.reshape(seq_count, length, count, 3, width // 3)
    flat = jnp.transpose(flat, (0, 2, 3, 1, 4))
    places = jnp.arange(length)
    allowed = (places[:, None] % local_cols == places[None, :] % local_cols) & (
        places[:, None] >= places[None, :]
    )
    result = attend(flat[:, :, 0], flat[:, :, 1], flat[:, :, 2], allowed)
    result = jnp.transpose(result, (0, 2, 1, 3)).reshape(
        seq_count, grid_rows, local_cols, count, width // 3
    )
    return lax.all_to_all(result, SEQ, split_axis=1, concat_axis=2, tiled=True)


def on_device(tokens, w_qkv, w_out):
    seq_count, tok_count, width = tokens.shape
    flat = tokens.reshape(seq_count * tok_count, width)
    half = HEADS // 2
    packed = w_out.reshape(w_qkv.shape[0], -1)
    both = jnp.concatenate([w_qkv, packed], axis=1)
    along_z = ring(both, "z", SIZE["z"])
    step = both.shape[1] // len(PARTS)
    spare = both.shape[1] - w_qkv.shape[1]
    pieces, tail = [], None
    for p, axes in enumerate(PARTS):
        own, other = with_other(rings(along_z[..., p * step:(p + 1) * step], axes))
        order = order_of(("z",) + axes)
        if p == len(PARTS) - 1:
            width = step - spare
            tail = (own[..., width:], other[..., width:]), order
            own, other = own[..., :width], other[..., :width]
        gathered = flat_rows((own, other), own.shape[-1])
        pieces.append(project(flat, w_qkv.shape[0], gathered, order))
    qkv = jnp.concatenate(pieces, axis=1).astype(jnp.bfloat16)
    (out_own, out_other), out_order = tail
    lead = out_own.shape[:-2]
    out_w = tuple(
        a.reshape(*lead, w_out.shape[0], w_out.shape[1]).reshape(-1, w_out.shape[1])
        for a in (out_own, out_other)
    )
    qkv = qkv.reshape(seq_count, tok_count, HEADS, 3, HEAD_DIM)
    col_packed = qkv[:, :, half:].reshape(seq_count, tok_count // COLS, COLS, half, 3 * HEAD_DIM)
    received = lax.all_to_all(col_packed, SEQ, split_axis=2, concat_axis=1, tiled=True)
    row_part = jnp.transpose(qkv[:, :, :half], (0, 2, 3, 1, 4))
    places = jnp.arange(tok_count)
    row_mask = (places[:, None] // COLS == places[None, :] // COLS) & (
        places[:, None] >= places[None, :]
    )
    row_out = attend(row_part[:, :, 0], row_part[:, :, 1], row_part[:, :, 2], row_mask)
    received, row_out = lax.optimization_barrier((received, row_out))
    col_out = column_heads(received).reshape(seq_count, tok_count, half, HEAD_DIM)
    row_out = jnp.transpose(row_out, (0, 2, 1, 3))
    heads_out = jnp.concatenate([row_out, col_out], axis=2).reshape(
        seq_count * tok_count, HEADS * HEAD_DIM
    )
    mixed = project(heads_out, w_out.shape[0], out_w, out_order)
    return mixed.astype(jnp.bfloat16).reshape(seq_count, tok_count, w_out.shape[1])


def solution(mesh):
    grid = Mesh(mesh.devices.reshape(SPLIT), AXES)
    act = P(("xh", "y"), SEQ, None)
    weight = P(AXES, None)
    return jax.shard_map(
        on_device, mesh=grid, in_specs=(act, weight, weight), out_specs=act, check_vma=False
    )
```

```python
import math

import jax
import jax.numpy as jnp
from jax import lax
from jax.sharding import Mesh
from jax.sharding import PartitionSpec as P

HEADS = 8
HEAD_DIM = 128
COLS = 96
AXES = ("xh", "y", "xl", "z", "c")
SPLIT = (2, 4, 2, 8, 2)
X = ("xh", "xl")
SEQ = ("xl", "z", "c")


def ring(block, axis, n):
    idx = lax.axis_index(axis)
    buf = jnp.zeros((n,) + block.shape, block.dtype)
    buf = lax.dynamic_update_index_in_dim(buf, block, idx, 0)
    fwd = bwd = block
    for s in range(1, n // 2 + 1):
        fwd = lax.ppermute(fwd, axis, [(i, (i + 1) % n) for i in range(n)])
        buf = lax.dynamic_update_index_in_dim(buf, fwd, (idx + n - s) % n, 0)
        if s < n - s:
            bwd = lax.ppermute(bwd, axis, [(i, (i - 1) % n) for i in range(n)])
            buf = lax.dynamic_update_index_in_dim(buf, bwd, (idx + s) % n, 0)
    return buf


DIMS = {"y": (2,), "z": (4,), X: (1, 3)}
SIZE = {"z": 8, "y": 4, X: 4}
PARTS = (("y", X), (X, "y"))


def rings(buf, axes):
    for axis in axes:
        buf = ring(buf, axis, SIZE[axis])
    return buf


def with_other(own):
    return own, lax.ppermute(own, "c", [(0, 1), (1, 0)])


def flat_rows(pair, cols):
    return tuple(a.reshape(-1, cols) for a in pair)


def order_of(axes):
    return tuple(reversed(axes))


def by_core(left, per_device, order):
    t = left.reshape(left.shape[0], *SPLIT, per_device)
    inner = tuple(d for axis in order for d in DIMS[axis])
    t = jnp.transpose(t, (0, 5) + inner + (6,))
    t = t.reshape(left.shape[0], 2, -1)
    c = lax.axis_index("c")
    own = lax.dynamic_index_in_dim(t, c, 1, keepdims=False)
    other = lax.dynamic_index_in_dim(t, 1 - c, 1, keepdims=False)
    return own, other


def project(left, per_device, gathered, order):
    own_w, other_w = gathered
    own, other = by_core(left, per_device, order)
    return jnp.dot(own, own_w, preferred_element_type=jnp.float32) + jnp.dot(
        other, other_w, preferred_element_type=jnp.float32
    )


def attend(query, keys, values, allowed):
    scores = jnp.einsum(
        "shqd,shkd->shqk", query, keys, preferred_element_type=jnp.float32
    ) / math.sqrt(query.shape[-1])
    scores = jnp.where(allowed, scores, -jnp.inf)
    top = jnp.max(scores, axis=-1, keepdims=True)
    expo = jnp.exp(scores - top)
    weights = (expo / jnp.sum(expo, axis=-1, keepdims=True)).astype(jnp.bfloat16)
    return jnp.einsum(
        "shqk,shkd->shqd", weights, values, preferred_element_type=jnp.float32
    ).astype(jnp.bfloat16)


def column_heads(packed):
    seq_count, grid_rows, local_cols, count, width = packed.shape
    length = grid_rows * local_cols
    flat = packed.reshape(seq_count, length, count, 3, width // 3)
    flat = jnp.transpose(flat, (0, 2, 3, 1, 4))
    places = jnp.arange(length)
    allowed = (places[:, None] % local_cols == places[None, :] % local_cols) & (
        places[:, None] >= places[None, :]
    )
    result = attend(flat[:, :, 0], flat[:, :, 1], flat[:, :, 2], allowed)
    result = jnp.transpose(result, (0, 2, 1, 3)).reshape(
        seq_count, grid_rows, local_cols, count, width // 3
    )
    return lax.all_to_all(result, SEQ, split_axis=1, concat_axis=2, tiled=True)


def on_device(tokens, w_qkv, w_out):
    seq_count, tok_count, width = tokens.shape
    flat = tokens.reshape(seq_count * tok_count, width)
    half = HEADS // 2
    packed = w_out.reshape(w_qkv.shape[0], -1)
    split = half * 3 * HEAD_DIM
    both = jnp.concatenate([w_qkv[:, split:], w_qkv[:, :split], packed], axis=1)
    along_z = ring(both, "z", SIZE["z"])
    bounds = ((0, w_qkv.shape[1] - split), (w_qkv.shape[1] - split, both.shape[1]))
    made = []
    for (lo, hi), axes in zip(bounds, PARTS):
        own, other = with_other(rings(along_z[..., lo:hi], axes))
        made.append(((own, other), order_of(("z",) + axes)))
    (col_own, col_other), col_order = made[0]
    col_w = flat_rows((col_own, col_other), col_own.shape[-1])
    col_qkv = project(flat, w_qkv.shape[0], col_w, col_order).astype(jnp.bfloat16)
    (rest_own, rest_other), out_order = made[1]
    row_w = flat_rows((rest_own[..., :split], rest_other[..., :split]), split)
    row_qkv = project(flat, w_qkv.shape[0], row_w, out_order).astype(jnp.bfloat16)
    lead = rest_own.shape[:-2]
    out_w = tuple(
        a[..., split:].reshape(*lead, w_out.shape[0], w_out.shape[1]).reshape(-1, w_out.shape[1])
        for a in (rest_own, rest_other)
    )
    col_packed = col_qkv.reshape(seq_count, tok_count // COLS, COLS, half, 3 * HEAD_DIM)
    received = lax.all_to_all(col_packed, SEQ, split_axis=2, concat_axis=1, tiled=True)
    row_part = row_qkv.reshape(seq_count, tok_count, half, 3, HEAD_DIM)
    row_part = jnp.transpose(row_part, (0, 2, 3, 1, 4))
    places = jnp.arange(tok_count)
    row_mask = (places[:, None] // COLS == places[None, :] // COLS) & (
        places[:, None] >= places[None, :]
    )
    row_out = attend(row_part[:, :, 0], row_part[:, :, 1], row_part[:, :, 2], row_mask)
    received, row_out = lax.optimization_barrier((received, row_out))
    col_out = column_heads(received).reshape(seq_count, tok_count, half, HEAD_DIM)
    row_out = jnp.transpose(row_out, (0, 2, 1, 3))
    heads_out = jnp.concatenate([row_out, col_out], axis=2).reshape(
        seq_count * tok_count, HEADS * HEAD_DIM
    )
    mixed = project(heads_out, w_out.shape[0], out_w, out_order)
    return mixed.astype(jnp.bfloat16).reshape(seq_count, tok_count, w_out.shape[1])


def solution(mesh):
    grid = Mesh(mesh.devices.reshape(SPLIT), AXES)
    act = P(("xh", "y"), SEQ, None)
    weight = P(AXES, None)
    return jax.shard_map(
        on_device, mesh=grid, in_specs=(act, weight, weight), out_specs=act, check_vma=False
    )
```

```python
import math

import jax
import jax.numpy as jnp
from jax import lax
from jax.sharding import Mesh
from jax.sharding import PartitionSpec as P

HEADS = 8
HEAD_DIM = 128
COLS = 96
AXES = ("xh", "y", "xl", "z", "c")
SPLIT = (2, 4, 2, 8, 2)
X = ("xh", "xl")
SEQ = ("xl", "z", "c")


def ring(block, axis, n):
    idx = lax.axis_index(axis)
    buf = jnp.zeros((n,) + block.shape, block.dtype)
    buf = lax.dynamic_update_index_in_dim(buf, block, idx, 0)
    fwd = bwd = block
    for s in range(1, n // 2 + 1):
        fwd = lax.ppermute(fwd, axis, [(i, (i + 1) % n) for i in range(n)])
        buf = lax.dynamic_update_index_in_dim(buf, fwd, (idx + n - s) % n, 0)
        if s < n - s:
            bwd = lax.ppermute(bwd, axis, [(i, (i - 1) % n) for i in range(n)])
            buf = lax.dynamic_update_index_in_dim(buf, bwd, (idx + s) % n, 0)
    return buf


DIMS = {"y": (2,), "z": (4,), X: (1, 3)}
SIZE = {"z": 8, "y": 4, X: 4}
PARTS = (("y", X), (X, "y"))


def rings(buf, axes):
    for axis in axes:
        buf = ring(buf, axis, SIZE[axis])
    return buf


def with_other(own):
    return own, lax.ppermute(own, "c", [(0, 1), (1, 0)])


def flat_rows(pair, cols):
    return tuple(a.reshape(-1, cols) for a in pair)


def order_of(axes):
    return tuple(reversed(axes))


def by_core(left, per_device, order):
    t = left.reshape(left.shape[0], *SPLIT, per_device)
    inner = tuple(d for axis in order for d in DIMS[axis])
    t = jnp.transpose(t, (0, 5) + inner + (6,))
    t = t.reshape(left.shape[0], 2, -1)
    c = lax.axis_index("c")
    own = lax.dynamic_index_in_dim(t, c, 1, keepdims=False)
    other = lax.dynamic_index_in_dim(t, 1 - c, 1, keepdims=False)
    return own, other


def project(left, per_device, gathered, order):
    own_w, other_w = gathered
    own, other = by_core(left, per_device, order)
    return jnp.dot(own, own_w, preferred_element_type=jnp.float32) + jnp.dot(
        other, other_w, preferred_element_type=jnp.float32
    )


def attend(query, keys, values, allowed):
    scores = jnp.einsum(
        "shqd,shkd->shqk", query, keys, preferred_element_type=jnp.float32
    ) / math.sqrt(query.shape[-1])
    scores = jnp.where(allowed, scores, -jnp.inf)
    top = jnp.max(scores, axis=-1, keepdims=True)
    expo = jnp.exp(scores - top)
    weights = (expo / jnp.sum(expo, axis=-1, keepdims=True)).astype(jnp.bfloat16)
    return jnp.einsum(
        "shqk,shkd->shqd", weights, values, preferred_element_type=jnp.float32
    ).astype(jnp.bfloat16)


def column_heads(packed):
    seq_count, grid_rows, local_cols, count, width = packed.shape
    length = grid_rows * local_cols
    flat = packed.reshape(seq_count, length, count, 3, width // 3)
    flat = jnp.transpose(flat, (0, 2, 3, 1, 4))
    places = jnp.arange(length)
    allowed = (places[:, None] % local_cols == places[None, :] % local_cols) & (
        places[:, None] >= places[None, :]
    )
    result = attend(flat[:, :, 0], flat[:, :, 1], flat[:, :, 2], allowed)
    result = jnp.transpose(result, (0, 2, 1, 3)).reshape(
        seq_count, grid_rows, local_cols, count, width // 3
    )
    return lax.all_to_all(result, SEQ, split_axis=1, concat_axis=2, tiled=True)


def on_device(tokens, w_qkv, w_out):
    seq_count, tok_count, width = tokens.shape
    flat = tokens.reshape(seq_count * tok_count, width)
    half = HEADS // 2
    packed = w_out.reshape(w_qkv.shape[0], -1)
    both = jnp.concatenate([w_qkv, packed], axis=1)
    spread = jnp.broadcast_to(both[None], (SIZE["z"],) + both.shape)
    along_z = lax.all_to_all(spread, "z", 0, 0, tiled=True)
    step = both.shape[1] // len(PARTS)
    spare = both.shape[1] - w_qkv.shape[1]
    pieces, tail = [], None
    for p, axes in enumerate(PARTS):
        own, other = with_other(rings(along_z[..., p * step:(p + 1) * step], axes))
        order = order_of(("z",) + axes)
        if p == len(PARTS) - 1:
            width = step - spare
            tail = (own[..., width:], other[..., width:]), order
            own, other = own[..., :width], other[..., :width]
        gathered = flat_rows((own, other), own.shape[-1])
        pieces.append(project(flat, w_qkv.shape[0], gathered, order))
    qkv = jnp.concatenate(pieces, axis=1).astype(jnp.bfloat16)
    (out_own, out_other), out_order = tail
    lead = out_own.shape[:-2]
    out_w = tuple(
        a.reshape(*lead, w_out.shape[0], w_out.shape[1]).reshape(-1, w_out.shape[1])
        for a in (out_own, out_other)
    )
    qkv = qkv.reshape(seq_count, tok_count, HEADS, 3, HEAD_DIM)
    col_packed = qkv[:, :, half:].reshape(seq_count, tok_count // COLS, COLS, half, 3 * HEAD_DIM)
    received = lax.all_to_all(col_packed, SEQ, split_axis=2, concat_axis=1, tiled=True)
    row_part = jnp.transpose(qkv[:, :, :half], (0, 2, 3, 1, 4))
    places = jnp.arange(tok_count)
    row_mask = (places[:, None] // COLS == places[None, :] // COLS) & (
        places[:, None] >= places[None, :]
    )
    row_out = attend(row_part[:, :, 0], row_part[:, :, 1], row_part[:, :, 2], row_mask)
    received, row_out = lax.optimization_barrier((received, row_out))
    col_out = column_heads(received).reshape(seq_count, tok_count, half, HEAD_DIM)
    row_out = jnp.transpose(row_out, (0, 2, 1, 3))
    heads_out = jnp.concatenate([row_out, col_out], axis=2).reshape(
        seq_count * tok_count, HEADS * HEAD_DIM
    )
    mixed = project(heads_out, w_out.shape[0], out_w, out_order)
    return mixed.astype(jnp.bfloat16).reshape(seq_count, tok_count, w_out.shape[1])


def solution(mesh):
    grid = Mesh(mesh.devices.reshape(SPLIT), AXES)
    act = P(("xh", "y"), SEQ, None)
    weight = P(AXES, None)
    return jax.shard_map(
        on_device, mesh=grid, in_specs=(act, weight, weight), out_specs=act, check_vma=False
    )
```

```python
import math

import jax
import jax.numpy as jnp
from jax import lax
from jax.sharding import Mesh
from jax.sharding import PartitionSpec as P

HEADS = 8
HEAD_DIM = 128
COLS = 96
AXES = ("xh", "y", "xl", "z", "c")
SPLIT = (2, 4, 2, 8, 2)
X = ("xh", "xl")
SEQ = ("xl", "z", "c")


def ring(block, axis, n):
    idx = lax.axis_index(axis)
    buf = jnp.zeros((n,) + block.shape, block.dtype)
    buf = lax.dynamic_update_index_in_dim(buf, block, idx, 0)
    fwd = bwd = block
    for s in range(1, n // 2 + 1):
        fwd = lax.ppermute(fwd, axis, [(i, (i + 1) % n) for i in range(n)])
        buf = lax.dynamic_update_index_in_dim(buf, fwd, (idx + n - s) % n, 0)
        if s < n - s:
            bwd = lax.ppermute(bwd, axis, [(i, (i - 1) % n) for i in range(n)])
            buf = lax.dynamic_update_index_in_dim(buf, bwd, (idx + s) % n, 0)
    return buf


DIMS = {"y": (2,), "z": (4,), X: (1, 3)}
SIZE = {"z": 8, "y": 4, X: 4}
PARTS = (("y", X), (X, "y"))


def rings(buf, axes):
    for axis in axes:
        buf = ring(buf, axis, SIZE[axis])
    return buf


def with_other(own):
    return own, lax.ppermute(own, "c", [(0, 1), (1, 0)])


def flat_rows(pair, cols):
    return tuple(a.reshape(-1, cols) for a in pair)


def order_of(axes):
    return tuple(reversed(axes))


def by_core(left, per_device, order):
    t = left.reshape(left.shape[0], *SPLIT, per_device)
    inner = tuple(d for axis in order for d in DIMS[axis])
    t = jnp.transpose(t, (0, 5) + inner + (6,))
    t = t.reshape(left.shape[0], 2, -1)
    c = lax.axis_index("c")
    own = lax.dynamic_index_in_dim(t, c, 1, keepdims=False)
    other = lax.dynamic_index_in_dim(t, 1 - c, 1, keepdims=False)
    return own, other


def project(left, per_device, gathered, order):
    own_w, other_w = gathered
    own, other = by_core(left, per_device, order)
    first = jnp.dot(own, own_w, preferred_element_type=jnp.float32)
    other_w, first = lax.optimization_barrier((other_w, first))
    return first + jnp.dot(other, other_w, preferred_element_type=jnp.float32)


def attend(query, keys, values, allowed):
    scores = jnp.einsum(
        "shqd,shkd->shqk", query, keys, preferred_element_type=jnp.float32
    ) / math.sqrt(query.shape[-1])
    scores = jnp.where(allowed, scores, -jnp.inf)
    top = jnp.max(scores, axis=-1, keepdims=True)
    expo = jnp.exp(scores - top)
    weights = (expo / jnp.sum(expo, axis=-1, keepdims=True)).astype(jnp.bfloat16)
    return jnp.einsum(
        "shqk,shkd->shqd", weights, values, preferred_element_type=jnp.float32
    ).astype(jnp.bfloat16)


def column_heads(packed):
    seq_count, grid_rows, local_cols, count, width = packed.shape
    length = grid_rows * local_cols
    flat = packed.reshape(seq_count, length, count, 3, width // 3)
    flat = jnp.transpose(flat, (0, 2, 3, 1, 4))
    places = jnp.arange(length)
    allowed = (places[:, None] % local_cols == places[None, :] % local_cols) & (
        places[:, None] >= places[None, :]
    )
    result = attend(flat[:, :, 0], flat[:, :, 1], flat[:, :, 2], allowed)
    result = jnp.transpose(result, (0, 2, 1, 3)).reshape(
        seq_count, grid_rows, local_cols, count, width // 3
    )
    return lax.all_to_all(result, SEQ, split_axis=1, concat_axis=2, tiled=True)


def on_device(tokens, w_qkv, w_out):
    seq_count, tok_count, width = tokens.shape
    flat = tokens.reshape(seq_count * tok_count, width)
    half = HEADS // 2
    packed = w_out.reshape(w_qkv.shape[0], -1)
    both = jnp.concatenate([w_qkv, packed], axis=1)
    spread = jnp.broadcast_to(both[None], (SIZE["z"],) + both.shape)
    along_z = lax.all_to_all(spread, "z", 0, 0, tiled=True)
    step = both.shape[1] // len(PARTS)
    spare = both.shape[1] - w_qkv.shape[1]
    pieces, tail = [], None
    for p, axes in enumerate(PARTS):
        own, other = with_other(rings(along_z[..., p * step:(p + 1) * step], axes))
        order = order_of(("z",) + axes)
        if p == len(PARTS) - 1:
            width = step - spare
            tail = (own[..., width:], other[..., width:]), order
            own, other = own[..., :width], other[..., :width]
        gathered = flat_rows((own, other), own.shape[-1])
        pieces.append(project(flat, w_qkv.shape[0], gathered, order))
    qkv = jnp.concatenate(pieces, axis=1).astype(jnp.bfloat16)
    (out_own, out_other), out_order = tail
    lead = out_own.shape[:-2]
    out_w = tuple(
        a.reshape(*lead, w_out.shape[0], w_out.shape[1]).reshape(-1, w_out.shape[1])
        for a in (out_own, out_other)
    )
    qkv = qkv.reshape(seq_count, tok_count, HEADS, 3, HEAD_DIM)
    col_packed = qkv[:, :, half:].reshape(seq_count, tok_count // COLS, COLS, half, 3 * HEAD_DIM)
    received = lax.all_to_all(col_packed, SEQ, split_axis=2, concat_axis=1, tiled=True)
    row_part = jnp.transpose(qkv[:, :, :half], (0, 2, 3, 1, 4))
    places = jnp.arange(tok_count)
    row_mask = (places[:, None] // COLS == places[None, :] // COLS) & (
        places[:, None] >= places[None, :]
    )
    row_out = attend(row_part[:, :, 0], row_part[:, :, 1], row_part[:, :, 2], row_mask)
    received, row_out = lax.optimization_barrier((received, row_out))
    col_out = column_heads(received).reshape(seq_count, tok_count, half, HEAD_DIM)
    row_out = jnp.transpose(row_out, (0, 2, 1, 3))
    heads_out = jnp.concatenate([row_out, col_out], axis=2).reshape(
        seq_count * tok_count, HEADS * HEAD_DIM
    )
    mixed = project(heads_out, w_out.shape[0], out_w, out_order)
    return mixed.astype(jnp.bfloat16).reshape(seq_count, tok_count, w_out.shape[1])


def solution(mesh):
    grid = Mesh(mesh.devices.reshape(SPLIT), AXES)
    act = P(("xh", "y"), SEQ, None)
    weight = P(AXES, None)
    return jax.shard_map(
        on_device, mesh=grid, in_specs=(act, weight, weight), out_specs=act, check_vma=False
    )
```

```python
import math

import jax
import jax.numpy as jnp
from jax import lax
from jax.sharding import Mesh
from jax.sharding import PartitionSpec as P

HEADS = 8
HEAD_DIM = 128
COLS = 96
AXES = ("xh", "y", "xl", "z", "c")
SPLIT = (2, 4, 2, 8, 2)
X = ("xh", "xl")
SEQ = ("xl", "z", "c")


def ring(block, axis, n):
    idx = lax.axis_index(axis)
    buf = jnp.zeros((n,) + block.shape, block.dtype)
    buf = lax.dynamic_update_index_in_dim(buf, block, idx, 0)
    fwd = bwd = block
    for s in range(1, n // 2 + 1):
        fwd = lax.ppermute(fwd, axis, [(i, (i + 1) % n) for i in range(n)])
        buf = lax.dynamic_update_index_in_dim(buf, fwd, (idx + n - s) % n, 0)
        if s < n - s:
            bwd = lax.ppermute(bwd, axis, [(i, (i - 1) % n) for i in range(n)])
            buf = lax.dynamic_update_index_in_dim(buf, bwd, (idx + s) % n, 0)
    return buf


DIMS = {"y": (2,), "z": (4,), X: (1, 3)}
SIZE = {"z": 8, "y": 4, X: 4}
PARTS = (("y", X), (X, "y"))


def rings(buf, axes):
    for axis in axes:
        buf = ring(buf, axis, SIZE[axis])
    return buf


def with_other(own):
    return own, lax.ppermute(own, "c", [(0, 1), (1, 0)])


def flat_rows(pair, cols):
    return tuple(a.reshape(-1, cols) for a in pair)


def order_of(axes):
    return tuple(reversed(axes))


def by_core(left, per_device, order):
    t = left.reshape(left.shape[0], *SPLIT, per_device)
    inner = tuple(d for axis in order for d in DIMS[axis])
    t = jnp.transpose(t, (0, 5) + inner + (6,))
    t = t.reshape(left.shape[0], 2, -1)
    c = lax.axis_index("c")
    own = lax.dynamic_index_in_dim(t, c, 1, keepdims=False)
    other = lax.dynamic_index_in_dim(t, 1 - c, 1, keepdims=False)
    return own, other


def project(left, per_device, gathered, order):
    own_w, other_w = gathered
    own, other = by_core(left, per_device, order)
    first = jnp.dot(own, own_w, preferred_element_type=jnp.float32)
    other_w, first = lax.optimization_barrier((other_w, first))
    return first + jnp.dot(other, other_w, preferred_element_type=jnp.float32)


def half_project(part, per_device, gathered):
    own_w, other_w = gathered
    t = part.reshape(part.shape[0], 1, *SPLIT[1:], per_device)
    t = jnp.transpose(t, (0, 5, 2, 1, 3, 4, 6)).reshape(part.shape[0], 2, -1)
    c = lax.axis_index("c")
    own = lax.dynamic_index_in_dim(t, c, 1, keepdims=False)
    other = lax.dynamic_index_in_dim(t, 1 - c, 1, keepdims=False)
    return jnp.dot(own, own_w, preferred_element_type=jnp.float32) + jnp.dot(
        other, other_w, preferred_element_type=jnp.float32
    )


def attend(query, keys, values, allowed):
    scores = jnp.einsum(
        "shqd,shkd->shqk", query, keys, preferred_element_type=jnp.float32
    ) / math.sqrt(query.shape[-1])
    scores = jnp.where(allowed, scores, -jnp.inf)
    top = jnp.max(scores, axis=-1, keepdims=True)
    expo = jnp.exp(scores - top)
    weights = (expo / jnp.sum(expo, axis=-1, keepdims=True)).astype(jnp.bfloat16)
    return jnp.einsum(
        "shqk,shkd->shqd", weights, values, preferred_element_type=jnp.float32
    ).astype(jnp.bfloat16)


def column_heads(packed):
    seq_count, grid_rows, local_cols, count, width = packed.shape
    length = grid_rows * local_cols
    flat = packed.reshape(seq_count, length, count, 3, width // 3)
    flat = jnp.transpose(flat, (0, 2, 3, 1, 4))
    places = jnp.arange(length)
    allowed = (places[:, None] % local_cols == places[None, :] % local_cols) & (
        places[:, None] >= places[None, :]
    )
    result = attend(flat[:, :, 0], flat[:, :, 1], flat[:, :, 2], allowed)
    result = jnp.transpose(result, (0, 2, 1, 3)).reshape(
        seq_count, grid_rows, local_cols, count, width // 3
    )
    return lax.all_to_all(result, SEQ, split_axis=1, concat_axis=2, tiled=True)


def on_device(tokens, w_qkv, w_out):
    seq_count, tok_count, width = tokens.shape
    flat = tokens.reshape(seq_count * tok_count, width)
    half = HEADS // 2
    packed = w_out.reshape(w_qkv.shape[0], -1)
    both = jnp.concatenate([w_qkv, packed], axis=1)
    spread = jnp.broadcast_to(both[None], (SIZE["z"],) + both.shape)
    along_z = lax.all_to_all(spread, "z", 0, 0, tiled=True)
    step = both.shape[1] // len(PARTS)
    spare = both.shape[1] - w_qkv.shape[1]
    pieces, tail = [], None
    for p, axes in enumerate(PARTS):
        own, other = with_other(rings(along_z[..., p * step:(p + 1) * step], axes))
        order = order_of(("z",) + axes)
        if p == len(PARTS) - 1:
            width = step - spare
            tail = (own[..., width:], other[..., width:]), order
            own, other = own[..., :width], other[..., :width]
        gathered = flat_rows((own, other), own.shape[-1])
        pieces.append(project(flat, w_qkv.shape[0], gathered, order))
    qkv = jnp.concatenate(pieces, axis=1).astype(jnp.bfloat16)
    (out_own, out_other), out_order = tail
    lead = out_own.shape[:-2]
    out_w = [a.reshape(*lead, w_out.shape[0], w_out.shape[1]) for a in (out_own, out_other)]
    split_x = SPLIT[AXES.index("xl")]
    row_w = tuple(a[:, :split_x].reshape(-1, w_out.shape[1]) for a in out_w)
    col_w = tuple(a[:, split_x:].reshape(-1, w_out.shape[1]) for a in out_w)
    qkv = qkv.reshape(seq_count, tok_count, HEADS, 3, HEAD_DIM)
    col_packed = qkv[:, :, half:].reshape(seq_count, tok_count // COLS, COLS, half, 3 * HEAD_DIM)
    received = lax.all_to_all(col_packed, SEQ, split_axis=2, concat_axis=1, tiled=True)
    row_part = jnp.transpose(qkv[:, :, :half], (0, 2, 3, 1, 4))
    places = jnp.arange(tok_count)
    row_mask = (places[:, None] // COLS == places[None, :] // COLS) & (
        places[:, None] >= places[None, :]
    )
    row_out = attend(row_part[:, :, 0], row_part[:, :, 1], row_part[:, :, 2], row_mask)
    received, row_out = lax.optimization_barrier((received, row_out))
    row_out = jnp.transpose(row_out, (0, 2, 1, 3)).reshape(seq_count * tok_count, half * HEAD_DIM)
    row_mixed = half_project(row_out, w_out.shape[0], row_w)
    col_out = column_heads(received)
    col_out, row_mixed = lax.optimization_barrier((col_out, row_mixed))
    col_out = col_out.reshape(seq_count * tok_count, half * HEAD_DIM)
    mixed = row_mixed + half_project(col_out, w_out.shape[0], col_w)
    return mixed.astype(jnp.bfloat16).reshape(seq_count, tok_count, w_out.shape[1])


def solution(mesh):
    grid = Mesh(mesh.devices.reshape(SPLIT), AXES)
    act = P(("xh", "y"), SEQ, None)
    weight = P(AXES, None)
    return jax.shard_map(
        on_device, mesh=grid, in_specs=(act, weight, weight), out_specs=act, check_vma=False
    )
```

```python
import math

import jax
import jax.numpy as jnp
from jax import lax
from jax.sharding import Mesh
from jax.sharding import PartitionSpec as P

HEADS = 8
HEAD_DIM = 128
COLS = 96
AXES = ("xh", "y", "xl", "z", "c")
SPLIT = (2, 4, 2, 8, 2)
X = ("xh", "xl")
SEQ = ("xl", "z", "c")


def ring(block, axis, n):
    idx = lax.axis_index(axis)
    buf = jnp.zeros((n,) + block.shape, block.dtype)
    buf = lax.dynamic_update_index_in_dim(buf, block, idx, 0)
    fwd = bwd = block
    for s in range(1, n // 2 + 1):
        fwd = lax.ppermute(fwd, axis, [(i, (i + 1) % n) for i in range(n)])
        buf = lax.dynamic_update_index_in_dim(buf, fwd, (idx + n - s) % n, 0)
        if s < n - s:
            bwd = lax.ppermute(bwd, axis, [(i, (i - 1) % n) for i in range(n)])
            buf = lax.dynamic_update_index_in_dim(buf, bwd, (idx + s) % n, 0)
    return buf


DIMS = {"y": (2,), "z": (4,), X: (1, 3)}
SIZE = {"z": 8, "y": 4, X: 4}
PARTS = (("y", X), (X, "y"))


def rings(buf, axes):
    for axis in axes:
        buf = ring(buf, axis, SIZE[axis])
    return buf


def with_other(own):
    return own, lax.ppermute(own, "c", [(0, 1), (1, 0)])


def flat_rows(pair, cols):
    return tuple(a.reshape(-1, cols) for a in pair)


def order_of(axes):
    return tuple(reversed(axes))


def by_core(left, per_device, order):
    t = left.reshape(left.shape[0], *SPLIT, per_device)
    inner = tuple(d for axis in order for d in DIMS[axis])
    t = jnp.transpose(t, (0, 5) + inner + (6,))
    t = t.reshape(left.shape[0], 2, -1)
    c = lax.axis_index("c")
    own = lax.dynamic_index_in_dim(t, c, 1, keepdims=False)
    other = lax.dynamic_index_in_dim(t, 1 - c, 1, keepdims=False)
    return own, other


def project(left, per_device, gathered, order):
    own_w, other_w = gathered
    own, other = by_core(left, per_device, order)
    first = jnp.dot(own, own_w, preferred_element_type=jnp.float32)
    other_w, first = lax.optimization_barrier((other_w, first))
    return first + jnp.dot(other, other_w, preferred_element_type=jnp.float32)


def attend(query, keys, values, allowed):
    scores = jnp.einsum(
        "shqd,shkd->shqk", query, keys, preferred_element_type=jnp.float32
    ) / math.sqrt(query.shape[-1])
    scores = jnp.where(allowed, scores, -jnp.inf)
    top = jnp.max(scores, axis=-1, keepdims=True)
    expo = jnp.exp(scores - top)
    weights = (expo / jnp.sum(expo, axis=-1, keepdims=True)).astype(jnp.bfloat16)
    return jnp.einsum(
        "shqk,shkd->shqd", weights, values, preferred_element_type=jnp.float32
    ).astype(jnp.bfloat16)


def column_heads(packed):
    seq_count, grid_rows, local_cols, count, width = packed.shape
    length = grid_rows * local_cols
    flat = packed.reshape(seq_count, length, count, 3, width // 3)
    flat = jnp.transpose(flat, (0, 2, 3, 1, 4))
    places = jnp.arange(length)
    allowed = (places[:, None] % local_cols == places[None, :] % local_cols) & (
        places[:, None] >= places[None, :]
    )
    result = attend(flat[:, :, 0], flat[:, :, 1], flat[:, :, 2], allowed)
    result = jnp.transpose(result, (0, 2, 1, 3)).reshape(
        seq_count, grid_rows, local_cols, count, width // 3
    )
    return lax.all_to_all(result, SEQ, split_axis=1, concat_axis=2, tiled=True)


def on_device(tokens, w_qkv, w_out):
    seq_count, tok_count, width = tokens.shape
    flat = tokens.reshape(seq_count * tok_count, width)
    half = HEADS // 2
    packed = w_out.reshape(w_qkv.shape[0], -1)
    both = jnp.concatenate([w_qkv, packed], axis=1)
    spread = jnp.broadcast_to(both[None], (SIZE["z"],) + both.shape)
    along_z = lax.all_to_all(spread, "z", 0, 0, tiled=True)
    step = both.shape[1] // len(PARTS)
    spare = both.shape[1] - w_qkv.shape[1]
    pieces, tail = [], None
    for p, axes in enumerate(PARTS):
        own, other = with_other(rings(along_z[..., p * step:(p + 1) * step], axes))
        order = order_of(("z",) + axes)
        if p == len(PARTS) - 1:
            width = step - spare
            tail = (own[..., width:], other[..., width:]), order
            own, other = own[..., :width], other[..., :width]
        gathered = flat_rows((own, other), own.shape[-1])
        pieces.append(project(flat, w_qkv.shape[0], gathered, order))
    qkv = jnp.concatenate(pieces, axis=1).astype(jnp.bfloat16)
    (out_own, out_other), out_order = tail
    lead = out_own.shape[:-2]
    out_w = tuple(
        a.reshape(*lead, w_out.shape[0], w_out.shape[1]).reshape(-1, w_out.shape[1])
        for a in (out_own, out_other)
    )
    qkv = qkv.reshape(seq_count, tok_count, HEADS, 3, HEAD_DIM)
    col_packed = qkv[:, :, half:].reshape(seq_count, tok_count // COLS, COLS, half, 3 * HEAD_DIM)
    chunks = 2
    per = half // chunks
    received = [
        lax.all_to_all(col_packed[:, :, :, k * per:(k + 1) * per], SEQ, split_axis=2, concat_axis=1, tiled=True)
        for k in range(chunks)
    ]
    row_part = jnp.transpose(qkv[:, :, :half], (0, 2, 3, 1, 4))
    places = jnp.arange(tok_count)
    row_mask = (places[:, None] // COLS == places[None, :] // COLS) & (
        places[:, None] >= places[None, :]
    )
    row_out = attend(row_part[:, :, 0], row_part[:, :, 1], row_part[:, :, 2], row_mask)
    first, row_out = lax.optimization_barrier((received[0], row_out))
    col_out = jnp.concatenate(
        [column_heads(first)] + [column_heads(r) for r in received[1:]], axis=3
    ).reshape(seq_count, tok_count, half, HEAD_DIM)
    row_out = jnp.transpose(row_out, (0, 2, 1, 3))
    heads_out = jnp.concatenate([row_out, col_out], axis=2).reshape(
        seq_count * tok_count, HEADS * HEAD_DIM
    )
    mixed = project(heads_out, w_out.shape[0], out_w, out_order)
    return mixed.astype(jnp.bfloat16).reshape(seq_count, tok_count, w_out.shape[1])


def solution(mesh):
    grid = Mesh(mesh.devices.reshape(SPLIT), AXES)
    act = P(("xh", "y"), SEQ, None)
    weight = P(AXES, None)
    return jax.shard_map(
        on_device, mesh=grid, in_specs=(act, weight, weight), out_specs=act, check_vma=False
    )
```

```python
import math

import jax
import jax.numpy as jnp
from jax import lax
from jax.sharding import Mesh
from jax.sharding import PartitionSpec as P

HEADS = 8
HEAD_DIM = 128
COLS = 96
AXES = ("xh", "y", "xl", "z", "c")
SPLIT = (2, 4, 2, 8, 2)
X = ("xh", "xl")
SEQ = ("xl", "z", "c")


def ring(block, axis, n):
    idx = lax.axis_index(axis)
    buf = jnp.zeros((n,) + block.shape, block.dtype)
    buf = lax.dynamic_update_index_in_dim(buf, block, idx, 0)
    fwd = bwd = block
    for s in range(1, n // 2 + 1):
        fwd = lax.ppermute(fwd, axis, [(i, (i + 1) % n) for i in range(n)])
        buf = lax.dynamic_update_index_in_dim(buf, fwd, (idx + n - s) % n, 0)
        if s < n - s:
            bwd = lax.ppermute(bwd, axis, [(i, (i - 1) % n) for i in range(n)])
            buf = lax.dynamic_update_index_in_dim(buf, bwd, (idx + s) % n, 0)
    return buf


DIMS = {"y": (2,), "z": (4,), X: (1, 3)}
SIZE = {"z": 8, "y": 4, X: 4}
PARTS = (("y", X), (X, "y"))


def rings(buf, axes):
    for axis in axes:
        buf = ring(buf, axis, SIZE[axis])
    return buf


def with_other(own):
    return own, lax.ppermute(own, "c", [(0, 1), (1, 0)])


def flat_rows(pair, cols):
    return tuple(a.reshape(-1, cols) for a in pair)


def order_of(axes):
    return tuple(reversed(axes))


def by_core(left, per_device, order):
    t = left.reshape(left.shape[0], *SPLIT, per_device)
    inner = tuple(d for axis in order for d in DIMS[axis])
    t = jnp.transpose(t, (0, 5) + inner + (6,))
    t = t.reshape(left.shape[0], 2, -1)
    c = lax.axis_index("c")
    own = lax.dynamic_index_in_dim(t, c, 1, keepdims=False)
    other = lax.dynamic_index_in_dim(t, 1 - c, 1, keepdims=False)
    return own, other


def project(left, per_device, gathered, order):
    own_w, other_w = gathered
    own, other = by_core(left, per_device, order)
    first = jnp.dot(own, own_w, preferred_element_type=jnp.float32)
    other_w, first = lax.optimization_barrier((other_w, first))
    return first + jnp.dot(other, other_w, preferred_element_type=jnp.float32)


def attend(query, keys, values, allowed):
    scores = jnp.einsum(
        "shqd,shkd->shqk", query, keys, preferred_element_type=jnp.float32
    ) / math.sqrt(query.shape[-1])
    scores = jnp.where(allowed, scores, -jnp.inf)
    top = jnp.max(scores, axis=-1, keepdims=True)
    expo = jnp.exp(scores - top)
    weights = (expo / jnp.sum(expo, axis=-1, keepdims=True)).astype(jnp.bfloat16)
    return jnp.einsum(
        "shqk,shkd->shqd", weights, values, preferred_element_type=jnp.float32
    ).astype(jnp.bfloat16)


def column_heads(packed):
    seq_count, grid_rows, local_cols, count, width = packed.shape
    length = grid_rows * local_cols
    flat = packed.reshape(seq_count, length, count, 3, width // 3)
    flat = jnp.transpose(flat, (0, 2, 3, 1, 4))
    places = jnp.arange(length)
    allowed = (places[:, None] % local_cols == places[None, :] % local_cols) & (
        places[:, None] >= places[None, :]
    )
    result = attend(flat[:, :, 0], flat[:, :, 1], flat[:, :, 2], allowed)
    result = jnp.transpose(result, (0, 2, 1, 3)).reshape(
        seq_count, grid_rows, local_cols, count, width // 3
    )
    return lax.all_to_all(result, SEQ, split_axis=1, concat_axis=2, tiled=True)


def on_device(tokens, w_qkv, w_out):
    seq_count, tok_count, width = tokens.shape
    flat = tokens.reshape(seq_count * tok_count, width)
    half = HEADS // 2
    packed = w_out.reshape(w_qkv.shape[0], -1)
    both = jnp.concatenate([w_qkv, packed], axis=1)
    spread = jnp.broadcast_to(both[None], (SIZE["z"],) + both.shape)
    along_z = lax.all_to_all(spread, "z", 0, 0, tiled=True)
    step = both.shape[1] // len(PARTS)
    spare = both.shape[1] - w_qkv.shape[1]
    pieces, tail = [], None
    for p, axes in enumerate(PARTS):
        own = rings(along_z[..., p * step:(p + 1) * step], axes)
        order = order_of(("z",) + axes)
        if p == len(PARTS) - 1:
            width = step - spare
            tail = own[..., width:], order
            own = own[..., :width]
        own, other = with_other(own)
        gathered = flat_rows((own, other), own.shape[-1])
        pieces.append(project(flat, w_qkv.shape[0], gathered, order))
    qkv = jnp.concatenate(pieces, axis=1).astype(jnp.bfloat16)
    out_own, out_order = tail
    out_own, qkv = lax.optimization_barrier((out_own, qkv))
    out_own, out_other = with_other(out_own)
    lead = out_own.shape[:-2]
    out_w = tuple(
        a.reshape(*lead, w_out.shape[0], w_out.shape[1]).reshape(-1, w_out.shape[1])
        for a in (out_own, out_other)
    )
    qkv = qkv.reshape(seq_count, tok_count, HEADS, 3, HEAD_DIM)
    col_packed = qkv[:, :, half:].reshape(seq_count, tok_count // COLS, COLS, half, 3 * HEAD_DIM)
    received = lax.all_to_all(col_packed, SEQ, split_axis=2, concat_axis=1, tiled=True)
    row_part = jnp.transpose(qkv[:, :, :half], (0, 2, 3, 1, 4))
    places = jnp.arange(tok_count)
    row_mask = (places[:, None] // COLS == places[None, :] // COLS) & (
        places[:, None] >= places[None, :]
    )
    row_out = attend(row_part[:, :, 0], row_part[:, :, 1], row_part[:, :, 2], row_mask)
    received, row_out = lax.optimization_barrier((received, row_out))
    col_out = column_heads(received).reshape(seq_count, tok_count, half, HEAD_DIM)
    row_out = jnp.transpose(row_out, (0, 2, 1, 3))
    heads_out = jnp.concatenate([row_out, col_out], axis=2).reshape(
        seq_count * tok_count, HEADS * HEAD_DIM
    )
    mixed = project(heads_out, w_out.shape[0], out_w, out_order)
    return mixed.astype(jnp.bfloat16).reshape(seq_count, tok_count, w_out.shape[1])


def solution(mesh):
    grid = Mesh(mesh.devices.reshape(SPLIT), AXES)
    act = P(("xh", "y"), SEQ, None)
    weight = P(AXES, None)
    return jax.shard_map(
        on_device, mesh=grid, in_specs=(act, weight, weight), out_specs=act, check_vma=False
    )
```

```python
import math

import jax
import jax.numpy as jnp
from jax import lax
from jax.sharding import Mesh
from jax.sharding import PartitionSpec as P

HEADS = 8
HEAD_DIM = 128
COLS = 96
AXES = ("xh", "y", "xl", "z", "c")
SPLIT = (2, 4, 2, 8, 2)
X = ("xh", "xl")
SEQ = ("xl", "z", "c")


def ring(block, axis, n):
    idx = lax.axis_index(axis)
    buf = jnp.zeros((n,) + block.shape, block.dtype)
    buf = lax.dynamic_update_index_in_dim(buf, block, idx, 0)
    fwd = bwd = block
    for s in range(1, n // 2 + 1):
        fwd = lax.ppermute(fwd, axis, [(i, (i + 1) % n) for i in range(n)])
        buf = lax.dynamic_update_index_in_dim(buf, fwd, (idx + n - s) % n, 0)
        if s < n - s:
            bwd = lax.ppermute(bwd, axis, [(i, (i - 1) % n) for i in range(n)])
            buf = lax.dynamic_update_index_in_dim(buf, bwd, (idx + s) % n, 0)
    return buf


DIMS = {"y": (2,), "z": (4,), X: (1, 3)}
SIZE = {"z": 8, "y": 4, X: 4}
PARTS = (("y", X), (X, "y"))


def rings(buf, axes):
    for axis in axes:
        buf = ring(buf, axis, SIZE[axis])
    return buf


def with_other(own):
    return own, lax.ppermute(own, "c", [(0, 1), (1, 0)])


def flat_rows(pair, cols):
    return tuple(a.reshape(-1, cols) for a in pair)


def order_of(axes):
    return tuple(reversed(axes))


def by_core(left, per_device, order):
    t = left.reshape(left.shape[0], *SPLIT, per_device)
    inner = tuple(d for axis in order for d in DIMS[axis])
    t = jnp.transpose(t, (0, 5) + inner + (6,))
    t = t.reshape(left.shape[0], 2, -1)
    c = lax.axis_index("c")
    own = lax.dynamic_index_in_dim(t, c, 1, keepdims=False)
    other = lax.dynamic_index_in_dim(t, 1 - c, 1, keepdims=False)
    return own, other


def project(left, per_device, gathered, order):
    own_w, other_w = gathered
    own, other = by_core(left, per_device, order)
    first = jnp.dot(own, own_w, preferred_element_type=jnp.float32)
    other_w, first = lax.optimization_barrier((other_w, first))
    return first + jnp.dot(other, other_w, preferred_element_type=jnp.float32)


def attend(query, keys, values, allowed):
    scores = jnp.einsum(
        "shqd,shkd->shqk", query, keys, preferred_element_type=jnp.float32
    ) / math.sqrt(query.shape[-1])
    scores = jnp.where(allowed, scores, -jnp.inf)
    top = jnp.max(scores, axis=-1, keepdims=True)
    expo = jnp.exp(scores - top)
    weights = (expo / jnp.sum(expo, axis=-1, keepdims=True)).astype(jnp.bfloat16)
    return jnp.einsum(
        "shqk,shkd->shqd", weights, values, preferred_element_type=jnp.float32
    ).astype(jnp.bfloat16)


def column_heads(packed):
    seq_count, grid_rows, local_cols, count, width = packed.shape
    length = grid_rows * local_cols
    flat = packed.reshape(seq_count, length, count, 3, width // 3)
    flat = jnp.transpose(flat, (0, 2, 3, 1, 4))
    places = jnp.arange(length)
    allowed = (places[:, None] % local_cols == places[None, :] % local_cols) & (
        places[:, None] >= places[None, :]
    )
    result = attend(flat[:, :, 0], flat[:, :, 1], flat[:, :, 2], allowed)
    result = jnp.transpose(result, (0, 2, 1, 3)).reshape(
        seq_count, grid_rows, local_cols, count, width // 3
    )
    return lax.all_to_all(result, SEQ, split_axis=1, concat_axis=2, tiled=True)


def on_device(tokens, w_qkv, w_out):
    seq_count, tok_count, width = tokens.shape
    flat = tokens.reshape(seq_count * tok_count, width)
    half = HEADS // 2
    packed = w_out.reshape(w_qkv.shape[0], -1)
    both = jnp.concatenate([w_qkv, packed], axis=1)
    spread = jnp.broadcast_to(both[None], (SIZE["z"],) + both.shape)
    along_z = lax.all_to_all(spread, "z", 0, 0, tiled=True)
    step = both.shape[1] // len(PARTS)
    spare = both.shape[1] - w_qkv.shape[1]
    pieces, tail = [], None
    for p, axes in enumerate(PARTS):
        own, other = with_other(rings(along_z[..., p * step:(p + 1) * step], axes))
        order = order_of(("z",) + axes)
        if p == len(PARTS) - 1:
            width = step - spare
            tail = (own[..., width:], other[..., width:]), order
            own, other = own[..., :width], other[..., :width]
        pieces.append((flat_rows((own, other), own.shape[-1]), order))
    split = half * 3 * HEAD_DIM
    (first_w, first_order), (second_w, second_order) = pieces
    col_qkv = jnp.concatenate(
        [
            project(flat, w_qkv.shape[0], tuple(a[:, split:] for a in first_w), first_order),
            project(flat, w_qkv.shape[0], second_w, second_order),
        ],
        axis=1,
    ).astype(jnp.bfloat16)
    row_qkv = project(
        flat, w_qkv.shape[0], tuple(a[:, :split] for a in first_w), first_order
    ).astype(jnp.bfloat16)
    (out_own, out_other), out_order = tail
    lead = out_own.shape[:-2]
    out_w = tuple(
        a.reshape(*lead, w_out.shape[0], w_out.shape[1]).reshape(-1, w_out.shape[1])
        for a in (out_own, out_other)
    )
    col_packed = col_qkv.reshape(seq_count, tok_count // COLS, COLS, half, 3 * HEAD_DIM)
    received = lax.all_to_all(col_packed, SEQ, split_axis=2, concat_axis=1, tiled=True)
    row_part = row_qkv.reshape(seq_count, tok_count, half, 3, HEAD_DIM)
    row_part = jnp.transpose(row_part, (0, 2, 3, 1, 4))
    places = jnp.arange(tok_count)
    row_mask = (places[:, None] // COLS == places[None, :] // COLS) & (
        places[:, None] >= places[None, :]
    )
    row_out = attend(row_part[:, :, 0], row_part[:, :, 1], row_part[:, :, 2], row_mask)
    received, row_out = lax.optimization_barrier((received, row_out))
    col_out = column_heads(received).reshape(seq_count, tok_count, half, HEAD_DIM)
    row_out = jnp.transpose(row_out, (0, 2, 1, 3))
    heads_out = jnp.concatenate([row_out, col_out], axis=2).reshape(
        seq_count * tok_count, HEADS * HEAD_DIM
    )
    mixed = project(heads_out, w_out.shape[0], out_w, out_order)
    return mixed.astype(jnp.bfloat16).reshape(seq_count, tok_count, w_out.shape[1])


def solution(mesh):
    grid = Mesh(mesh.devices.reshape(SPLIT), AXES)
    act = P(("xh", "y"), SEQ, None)
    weight = P(AXES, None)
    return jax.shard_map(
        on_device, mesh=grid, in_specs=(act, weight, weight), out_specs=act, check_vma=False
    )
```
